32 devices in a mesh: groups: 2 (over x), seq: 16 (over z, y, core).
Axes of the slice: x: 2, y: 2, z: 4, core: 2. Of those that a mesh axis runs over, the one named last changes fastest.
Arguments:
- queries: bfloat16 [12288, 1536], P(('groups', 'seq')), parts along dimension 0, may hold values from -6 to 6
- keys: bfloat16 [12288, 1536], P(('groups', 'seq')), parts along dimension 0, may hold values from -6 to 6
- values: bfloat16 [12288, 1536], P(('groups', 'seq')), parts along dimension 0, may hold values from -6 to 6
- tile_lengths: int32 [32], P(('groups', 'seq')), parts along dimension 0, may hold values from 192 to 384
- head_windows: int32 [12, 2], replicated, may hold values from 0 to 1
- out_weight: bfloat16 [1536, 3072], P('seq'), may hold values from -0.4375 to 0.4375
- gate: float32 [6144], P('groups'), parts along dimension 0, may hold values from 0.5 to 2
Outputs:
- attn_branch: bfloat16 [12288, 3072], P(('groups', 'seq')), parts along dimension 0
The draws below stay inside these ranges and needn't reach their ends.
There are 2 independent parts, one for each index of `groups`. The reference program is written for one: setup_inputs(seed, part) draws one part's arguments, and reference() takes and returns one part's arrays. A program takes and returns all parts, laid end to end along the dimension named above; an argument that names none is the same for every part. Nothing has to cross between parts.
All inputs are finite; a program needn't handle non-finite values.
Results may differ from the reference program's by a relative error of at most 0.0057.
Values may be sent and summed in bfloat16 or wider, within the bound.
No kernel may reach another device: no remote copies, remote signals or barrier semaphores. Data moves between devices by JAX's collectives and lax.ppermute only.
A program may use at most 128 MiB of HBM per device.

```python
import math
import jax
import jax.numpy as jnp
from jax import lax

D = 3072
HEADS = 12
HD = 128
TILE = 384
TW = 8
TILES = 16
TOKENS = 6144
HH = 1536


def shared_rows(key):
    base = jax.random.fold_in(key, 7)
    width = HEADS * HD
    in_tile = jnp.arange(TOKENS, dtype=jnp.int32) % TILE
    strength = jnp.zeros((TOKENS,), jnp.float32)
    leader = jnp.zeros((TOKENS,), jnp.float32)
    follower = jnp.zeros((TOKENS,), jnp.bool_)
    for first, level in ((TILE // 48, 3.0), (TILE // 6, 3.8), (TILE * 2 // 5, 4.5)):
        strength = jnp.where(in_tile == first, level, strength)
        strength = jnp.where(in_tile == first + 1, 0.99 * level, strength)
        leader = jnp.where(in_tile == first, level, leader)
        follower = follower | (in_tile == first + 1)
    keys_out = jnp.clip(jax.random.normal(jax.random.fold_in(base, 5), (TOKENS, width), jnp.float32), -4.5, 4.5)
    queries_out = jnp.clip(1.5 * jax.random.normal(jax.random.fold_in(base, 6), (TOKENS, width), jnp.float32), -5.5, 5.5)
    return (queries_out, keys_out)


def draw_queries(key, part):
    queries_out, keys_out = shared_rows(key)
    return queries_out.astype(jnp.bfloat16)


def draw_keys(key, part):
    queries_out, keys_out = shared_rows(key)
    return keys_out.astype(jnp.bfloat16)


def touch_ends(drawn, own_key, smallest, top_value):
    longest = drawn.shape.index(max(drawn.shape))
    spots = []
    for shift in (0, 1):
        where = [jax.random.randint(jax.random.fold_in(own_key, axis), (), 0, length) for axis, length in enumerate(drawn.shape)]
        where[longest] = (where[longest] + shift) % drawn.shape[longest]
        spots.append(tuple(where))
    return drawn.at[spots[0]].set(smallest).at[spots[1]].set(top_value)


def levels(rng, dims, split, low, largest):
    def one(dim, blocks):
        steps = jax.random.uniform(jax.random.fold_in(jax.random.fold_in(rng, 6), dim), (blocks,), jnp.float32, low / len(split), largest / len(split))
        return jnp.repeat(jnp.exp(steps), dims[dim] // blocks).reshape((-1,) + (1,) * (len(dims) - dim - 1))

    factor_of = one(*split[0])
    for cut in split[1:]:
        factor_of = factor_of * one(*cut)
    return factor_of


def normal_values(key, extent, spread, bound, split=(), kind=jnp.bfloat16):
    level = levels(key, extent, split, -0.22, 0.18) if split else 1.0
    result = jax.random.normal(key, extent, jnp.float32) * spread * level
    return jnp.minimum(jnp.maximum(result, -bound), bound).astype(kind)


def setup_inputs(seed: int = 0, part: int = 0) -> dict:
    arg_keys = jax.random.split(jax.random.key(seed), 8)
    part_splits = jax.random.split(jax.random.fold_in(arg_keys[7], part), 8)
    return {
        "queries": draw_queries(jax.random.fold_in(jax.random.fold_in(arg_keys[7], part), 71), part),
        "keys": draw_keys(jax.random.fold_in(jax.random.fold_in(arg_keys[7], part), 71), part),
        "values": normal_values(part_splits[2], (TOKENS, HH), 1.0, 6.0, ((0, 16),)),
        "tile_lengths": touch_ends(jax.random.randint(part_splits[3], (TILES,), TILE // 2, TILE + 1), jax.random.fold_in(part_splits[3], 1), TILE // 2, TILE).astype(jnp.int32),
        "head_windows": touch_ends(jax.random.randint(arg_keys[4], (HEADS, 2), 0, 2), jax.random.fold_in(arg_keys[4], 1), 0, 1).astype(jnp.int32),
        "out_weight": normal_values(arg_keys[5], (HH, D), (HEADS * HD // 9) ** -0.5, 0.4375, ((0, 16),)),
        "gate": jnp.clip(jax.random.uniform(part_splits[6], (D,), jnp.float32, 0.5, 2.0), 0.5, 2.0),
    }


def reference(queries, keys, values, tile_lengths, head_windows, out_weight, gate):
    score_scale = 1.0 / math.sqrt(HD)
    grid_rows = TILES // TW
    row_steps = jnp.array([-1, -1, -1, 0, 0, 0, 1, 1, 1], jnp.int32)
    col_steps = jnp.array([-1, 0, 1, -1, 0, 1, -1, 0, 1], jnp.int32)
    positions = jnp.arange(TILE, dtype=jnp.int32)

    def take_tile(source, number):
        return lax.dynamic_slice_in_dim(source, (number * TILE).astype(jnp.int32), TILE, 0)

    def one_tile(number):
        grid_row = number // TW
        grid_col = number % TW
        near_rows = grid_row + row_steps
        near_cols = grid_col + col_steps
        inside = (near_rows >= 0) & (near_rows < grid_rows) & (near_cols >= 0) & (near_cols < TW)
        near_tiles = (jnp.clip(near_rows, 0, grid_rows - 1) * TW + jnp.clip(near_cols, 0, TW - 1)).astype(jnp.int32)
        key_stack = jax.vmap(lambda neighbour: take_tile(keys, neighbour))(near_tiles)
        value_stack = jax.vmap(lambda neighbour: take_tile(values, neighbour))(near_tiles)
        near_lengths = jnp.where(inside, tile_lengths[near_tiles], 0)
        query_block = take_tile(queries, number).astype(jnp.float32).reshape(TILE, HEADS, HD)
        key_block = key_stack.astype(jnp.float32).reshape(9, TILE, HEADS, HD)
        scores = jnp.einsum('qhd,okhd->hqok', query_block, key_block) * score_scale
        key_real = positions[None, :] < near_lengths[:, None]
        window = (jnp.abs(row_steps)[None, :] <= head_windows[:, 0:1]) & (jnp.abs(col_steps)[None, :] <= head_windows[:, 1:2])
        allowed = (window[:, :, None] & key_real[None, :, :]).reshape(HEADS, 1, 9 * TILE)
        scores = scores.reshape(HEADS, TILE, 9 * TILE)
        scores = jnp.where(allowed, scores, -1e+30)
        maximum = lax.optimization_barrier(jnp.max(scores, axis=2, keepdims=True))
        exponent = jnp.where(allowed, jnp.exp(scores - maximum), 0.0)
        denominator = lax.optimization_barrier(jnp.sum(exponent, axis=2, keepdims=True))
        weights = (exponent / denominator).astype(jnp.bfloat16)
        value_block = value_stack.astype(jnp.float32).reshape(9 * TILE, HEADS, HD)
        attended = jnp.einsum('hqk,khd->qhd', weights.astype(jnp.float32), value_block)
        query_real = positions < tile_lengths[number]
        attended = jnp.where(query_real[:, None, None], attended, 0.0)
        return attended.reshape(TILE, HEADS * HD).astype(jnp.bfloat16)
    attended_all = lax.map(one_tile, jnp.arange(TILES, dtype=jnp.int32)).reshape(TOKENS, HEADS * HD)
    projected = jnp.dot(attended_all, out_weight, preferred_element_type=jnp.float32)
    return (projected * gate[None, :]).astype(jnp.bfloat16)
```

```python
import math

import jax
import jax.numpy as jnp
from jax import lax
from jax.sharding import PartitionSpec as P

TW = 8


def attend(query_block, head_keys, head_values, usable, score_scale):
    scores = (
        lax.dot_general(
            query_block, head_keys, (((1,), (1,)), ((), ())), preferred_element_type=jnp.float32
        )
        * score_scale
    )
    scores = jnp.where(usable[None, :], scores, -1e30)
    maximum = jnp.max(scores, axis=1, keepdims=True)
    exponent = jnp.where(usable[None, :], jnp.exp(scores - maximum), 0.0)
    denominator = jnp.sum(exponent, axis=1, keepdims=True)
    weights = (exponent / denominator).astype(jnp.bfloat16)
    return jnp.dot(weights, head_values, preferred_element_type=jnp.float32)


def vertical_parts(devices, grid_rows):
    if grid_rows == 1:
        return []
    down = [(i, i + TW) for i in range(devices - TW)]
    up = [(i + TW, i) for i in range(devices - TW)]
    if grid_rows == 2:
        return [down + up]
    return [down, up]


def on_device(queries, keys, values, tile_lengths, head_windows, out_weight, gate):
    devices = lax.axis_size("seq")
    grid_rows = devices // TW
    tile_rows = queries.shape[0]
    feat_width = queries.shape[1]
    head_count = head_windows.shape[0]
    head_dim = feat_width // head_count
    score_scale = 1.0 / math.sqrt(head_dim)

    pair = jnp.concatenate([keys, values], axis=1)
    column = [pair]
    column_lengths = [tile_lengths]
    column_rows = [0]
    for pairs in vertical_parts(devices, grid_rows):
        got, got_lengths = lax.ppermute((pair, tile_lengths), "seq", pairs)
        column.append(got)
        column_lengths.append(got_lengths)
        column_rows.append(1)
    column = jnp.stack(column)
    column_lengths = jnp.concatenate(column_lengths)

    to_right = [(i, i + 1) for i in range(devices) if i % TW < TW - 1]
    to_left = [(i + 1, i) for i in range(devices) if i % TW < TW - 1]
    from_left = lax.ppermute((column, column_lengths), "seq", to_right)
    from_right = lax.ppermute((column, column_lengths), "seq", to_left)

    slots = len(column_rows)
    key_stack = jnp.concatenate([column, from_left[0], from_right[0]])
    length_stack = jnp.concatenate([column_lengths, from_left[1], from_right[1]])
    far_rows = jnp.array(column_rows * 3, jnp.int32)
    far_cols = jnp.array([0] * slots + [1] * slots + [1] * slots, jnp.int32)
    key_flat = key_stack.reshape(3 * slots * tile_rows, 2 * feat_width)

    positions = jnp.arange(tile_rows, dtype=jnp.int32)
    key_real = positions[None, :] < length_stack[:, None]
    query_real = positions < tile_lengths[0]

    def one_head(head_index, attended_all):
        offset = head_index * head_dim
        query_block = lax.dynamic_slice_in_dim(queries, offset, head_dim, 1)
        head_keys = lax.dynamic_slice_in_dim(key_flat, offset, head_dim, 1)
        head_values = lax.dynamic_slice_in_dim(key_flat, feat_width + offset, head_dim, 1)
        reach_rows = head_windows[head_index, 0]
        reach_cols = head_windows[head_index, 1]
        window = (far_rows <= reach_rows) & (far_cols <= reach_cols)
        usable = (key_real & window[:, None]).reshape(-1)
        attended = attend(query_block, head_keys, head_values, usable, score_scale)
        attended = jnp.where(query_real[:, None], attended, 0.0).astype(jnp.bfloat16)
        return lax.dynamic_update_slice_in_dim(attended_all, attended, offset, 1)

    attended_all = lax.fori_loop(
        0, head_count, one_head, jnp.zeros((tile_rows, feat_width), jnp.bfloat16)
    )
    projected = jnp.dot(
        attended_all,
        lax.all_gather(out_weight, "seq", axis=0, tiled=True),
        preferred_element_type=jnp.float32,
    )
    return (projected * gate[None, :]).astype(jnp.bfloat16)


def solution(mesh):
    placed = (
        P(("groups", "seq"), None),
        P(("groups", "seq"), None),
        P(("groups", "seq"), None),
        P(("groups", "seq")),
        P(),
        P("seq", None),
        P("groups"),
    )
    return jax.shard_map(
        on_device, mesh=mesh, in_specs=placed, out_specs=P(("groups", "seq"), None), check_vma=False
    )
```

```python
import math

import jax
import jax.numpy as jnp
from jax import lax
from jax.sharding import PartitionSpec as P

TW = 8
GROUPS = 4


def attend(query_block, head_keys, head_values, usable, score_scale):
    scores = (
        lax.dot_general(
            query_block, head_keys, (((1,), (1,)), ((), ())), preferred_element_type=jnp.float32
        )
        * score_scale
    )
    scores = jnp.where(usable[None, :], scores, -1e30)
    maximum = jnp.max(scores, axis=1, keepdims=True)
    exponent = jnp.where(usable[None, :], jnp.exp(scores - maximum), 0.0)
    denominator = jnp.sum(exponent, axis=1, keepdims=True)
    weights = (exponent / denominator).astype(jnp.bfloat16)
    return jnp.dot(weights, head_values, preferred_element_type=jnp.float32)


def vertical_parts(devices, grid_rows):
    if grid_rows == 1:
        return []
    down = [(i, i + TW) for i in range(devices - TW)]
    up = [(i + TW, i) for i in range(devices - TW)]
    if grid_rows == 2:
        return [down + up]
    return [down, up]


def on_device(queries, keys, values, tile_lengths, head_windows, out_weight, gate):
    devices = lax.axis_size("seq")
    grid_rows = devices // TW
    tile_rows = queries.shape[0]
    feat_width = queries.shape[1]
    head_count = head_windows.shape[0]
    head_dim = feat_width // head_count
    score_scale = 1.0 / math.sqrt(head_dim)
    groups = GROUPS if head_count % GROUPS == 0 else 1
    group_heads = head_count // groups
    group_width = group_heads * head_dim

    to_right = [(i, i + 1) for i in range(devices) if i % TW < TW - 1]
    to_left = [(i + 1, i) for i in range(devices) if i % TW < TW - 1]
    sideways = lambda x: (lax.ppermute(x, "seq", to_right), lax.ppermute(x, "seq", to_left))

    weight_all = lax.all_gather(out_weight, "seq", axis=0, tiled=True)
    (left_k, left_v, left_len), (right_k, right_v, right_len) = sideways(
        (keys, values, tile_lengths)
    )
    verticals = vertical_parts(devices, grid_rows)

    positions = jnp.arange(tile_rows, dtype=jnp.int32)
    query_real = positions < tile_lengths[0]

    def chunk(x, g):
        return lax.slice_in_dim(x, g * group_width, (g + 1) * group_width, axis=1)

    outputs = []
    previous = None
    for g in range(groups):
        own = jnp.concatenate([chunk(keys, g), chunk(values, g)], axis=1)
        if previous is not None:
            own, _ = lax.optimization_barrier((own, previous))
        got = [lax.ppermute((own, tile_lengths), "seq", pairs) for pairs in verticals]
        if got:
            previous = got[-1][0]
        forwarded = [sideways(item) for item in got]
        slots = [own]
        lengths = [tile_lengths]
        rows = [0]
        cols = [0]
        for item in got:
            slots.append(item[0])
            lengths.append(item[1])
            rows.append(1)
            cols.append(0)
        slots += [jnp.concatenate([chunk(left_k, g), chunk(left_v, g)], axis=1),
                  jnp.concatenate([chunk(right_k, g), chunk(right_v, g)], axis=1)]
        lengths += [left_len, right_len]
        rows += [0, 0]
        cols += [1, 1]
        for from_left, from_right in forwarded:
            slots += [from_left[0], from_right[0]]
            lengths += [from_left[1], from_right[1]]
            rows += [1, 1]
            cols += [1, 1]
        key_flat = jnp.concatenate(slots)
        length_stack = jnp.concatenate(lengths)
        key_real = positions[None, :] < length_stack[:, None]
        far_rows = jnp.array(rows, jnp.int32)
        far_cols = jnp.array(cols, jnp.int32)
        for j in range(group_heads):
            head_index = g * group_heads + j
            offset = j * head_dim
            query_block = lax.slice_in_dim(
                queries, head_index * head_dim, (head_index + 1) * head_dim, axis=1
            )
            head_keys = lax.slice_in_dim(key_flat, offset, offset + head_dim, axis=1)
            head_values = lax.slice_in_dim(
                key_flat, group_width + offset, group_width + offset + head_dim, axis=1
            )
            window = (far_rows <= head_windows[head_index, 0]) & (
                far_cols <= head_windows[head_index, 1]
            )
            usable = (key_real & window[:, None]).reshape(-1)
            attended = attend(query_block, head_keys, head_values, usable, score_scale)
            outputs.append(jnp.where(query_real[:, None], attended, 0.0).astype(jnp.bfloat16))

    attended_all = jnp.concatenate(outputs, axis=1)
    projected = jnp.dot(attended_all, weight_all, preferred_element_type=jnp.float32)
    return (projected * gate[None, :]).astype(jnp.bfloat16)


def solution(mesh):
    placed = (
        P(("groups", "seq"), None),
        P(("groups", "seq"), None),
        P(("groups", "seq"), None),
        P(("groups", "seq")),
        P(),
        P("seq", None),
        P("groups"),
    )
    return jax.shard_map(
        on_device, mesh=mesh, in_specs=placed, out_specs=P(("groups", "seq"), None), check_vma=False
    )
```

```python
import math

import jax
import jax.numpy as jnp
from jax import lax
from jax.experimental import pallas as pl
from jax.sharding import PartitionSpec as P

TW = 8
GROUPS = 4


def group_attention(queries, slots, usable, head_base, group_heads, head_dim, score_scale):
    tile_rows, feat_width = queries.shape
    count = len(slots)

    def kernel(*refs):
        query = refs[0][...]
        key_refs = refs[1:1 + 2 * count:2]
        value_refs = refs[2:2 + 2 * count:2]
        mask_ref = refs[1 + 2 * count]
        out_ref = refs[-1]
        scores = []
        allowed = []
        for j in range(count):
            part = lax.dot_general(
                query, key_refs[j][...], (((1,), (1,)), ((), ())),
                preferred_element_type=jnp.float32,
            ) * score_scale
            ok = mask_ref[0, j:j + 1, :] != 0
            scores.append(jnp.where(ok, part, -1e30))
            allowed.append(ok)
        maximum = scores[0].max(axis=1, keepdims=True)
        for part in scores[1:]:
            maximum = jnp.maximum(maximum, part.max(axis=1, keepdims=True))
        exponents = [
            jnp.where(ok, jnp.exp(part - maximum), 0.0) for part, ok in zip(scores, allowed)
        ]
        denominator = exponents[0].sum(axis=1, keepdims=True)
        for part in exponents[1:]:
            denominator = denominator + part.sum(axis=1, keepdims=True)
        total = None
        for j in range(count):
            weights = (exponents[j] / denominator).astype(jnp.bfloat16)
            term = jnp.dot(weights, value_refs[j][...], preferred_element_type=jnp.float32)
            total = term if total is None else total + term
        out_ref[...] = total.astype(out_ref.dtype)

    in_specs = [pl.BlockSpec((tile_rows, head_dim), lambda h: (0, head_base + h))]
    operands = [queries]
    for key_array, value_array, key_block, value_block in slots:
        in_specs.append(pl.BlockSpec((tile_rows, head_dim), lambda h, b=key_block: (0, b + h)))
        in_specs.append(pl.BlockSpec((tile_rows, head_dim), lambda h, b=value_block: (0, b + h)))
        operands += [key_array, value_array]
    in_specs.append(pl.BlockSpec((1, count, tile_rows), lambda h: (h, 0, 0)))
    operands.append(usable.astype(jnp.int32))
    return pl.pallas_call(
        kernel,
        grid=(group_heads,),
        in_specs=in_specs,
        out_specs=pl.BlockSpec((tile_rows, head_dim), lambda h: (0, h)),
        out_shape=jax.ShapeDtypeStruct((tile_rows, group_heads * head_dim), queries.dtype),
    )(*operands)


def vertical_parts(devices, grid_rows):
    if grid_rows == 1:
        return []
    down = [(i, i + TW) for i in range(devices - TW)]
    up = [(i + TW, i) for i in range(devices - TW)]
    if grid_rows == 2:
        return [down + up]
    return [down, up]


def on_device(queries, keys, values, tile_lengths, head_windows, out_weight, gate):
    devices = lax.axis_size("seq")
    grid_rows = devices // TW
    tile_rows = queries.shape[0]
    feat_width = queries.shape[1]
    head_count = head_windows.shape[0]
    head_dim = feat_width // head_count
    score_scale = 1.0 / math.sqrt(head_dim)
    groups = GROUPS if head_count % GROUPS == 0 else 1
    group_heads = head_count // groups
    group_width = group_heads * head_dim

    to_right = [(i, i + 1) for i in range(devices) if i % TW < TW - 1]
    to_left = [(i + 1, i) for i in range(devices) if i % TW < TW - 1]
    sideways = lambda x: (lax.ppermute(x, "seq", to_right), lax.ppermute(x, "seq", to_left))

    weight_all = lax.all_gather(out_weight, "seq", axis=0, tiled=True)
    (left_k, left_v, left_len), (right_k, right_v, right_len) = sideways(
        (keys, values, tile_lengths)
    )
    verticals = vertical_parts(devices, grid_rows)

    positions = jnp.arange(tile_rows, dtype=jnp.int32)
    query_real = positions < tile_lengths[0]

    def chunk(x, g):
        return lax.slice_in_dim(x, g * group_width, (g + 1) * group_width, axis=1)

    outputs = []
    previous = None
    for g in range(groups):
        own = jnp.concatenate([chunk(keys, g), chunk(values, g)], axis=1)
        if previous is not None:
            own, _ = lax.optimization_barrier((own, previous))
        got = [lax.ppermute((own, tile_lengths), "seq", pairs) for pairs in verticals]
        if got:
            previous = got[-1][0]
        forwarded = [sideways(item) for item in got]
        base = g * group_heads
        slots = [(keys, values, base, base)]
        lengths = [tile_lengths]
        rows = [0]
        cols = [0]
        for item in got:
            slots.append((item[0], item[0], 0, group_heads))
            lengths.append(item[1])
            rows.append(1)
            cols.append(0)
        slots += [(left_k, left_v, base, base), (right_k, right_v, base, base)]
        lengths += [left_len, right_len]
        rows += [0, 0]
        cols += [1, 1]
        for from_left, from_right in forwarded:
            slots += [(from_left[0], from_left[0], 0, group_heads),
                      (from_right[0], from_right[0], 0, group_heads)]
            lengths += [from_left[1], from_right[1]]
            rows += [1, 1]
            cols += [1, 1]
        length_stack = jnp.concatenate(lengths)
        key_real = positions[None, :] < length_stack[:, None]
        far_rows = jnp.array(rows, jnp.int32)
        far_cols = jnp.array(cols, jnp.int32)
        reach = lax.slice_in_dim(head_windows, base, base + group_heads, axis=0)
        window = (far_rows[None, :] <= reach[:, 0:1]) & (far_cols[None, :] <= reach[:, 1:2])
        usable = key_real[None, :, :] & window[:, :, None]
        attended = group_attention(
            queries, slots, usable, base, group_heads, head_dim, score_scale
        )
        outputs.append(jnp.where(query_real[:, None], attended, 0))

    attended_all = jnp.concatenate(outputs, axis=1)
    projected = jnp.dot(attended_all, weight_all, preferred_element_type=jnp.float32)
    return (projected * gate[None, :]).astype(jnp.bfloat16)


def solution(mesh):
    placed = (
        P(("groups", "seq"), None),
        P(("groups", "seq"), None),
        P(("groups", "seq"), None),
        P(("groups", "seq")),
        P(),
        P("seq", None),
        P("groups"),
    )
    return jax.shard_map(
        on_device, mesh=mesh, in_specs=placed, out_specs=P(("groups", "seq"), None), check_vma=False
    )
```

```python
import math

import jax
import jax.numpy as jnp
from jax import lax
from jax.experimental import pallas as pl
from jax.sharding import PartitionSpec as P


TW = 8
GROUPS = 4


def group_attention(queries, slots, usable, head_base, group_heads, head_dim, score_scale):
    tile_rows, _ = queries.shape
    count = len(slots)

    def kernel(*refs):
        query = refs[0][...]
        key_refs = refs[1:1 + 2 * count:2]
        value_refs = refs[2:2 + 2 * count:2]
        mask_ref = refs[1 + 2 * count]
        out_ref = refs[-1]
        scores = []
        allowed = []
        for j in range(count):
            part = lax.dot_general(
                query, key_refs[j][...], (((1,), (1,)), ((), ())),
                preferred_element_type=jnp.float32,
            ) * score_scale
            ok = mask_ref[0, j:j + 1, :] != 0
            scores.append(jnp.where(ok, part, -1e30))
            allowed.append(ok)
        maximum = scores[0].max(axis=1, keepdims=True)
        for part in scores[1:]:
            maximum = jnp.maximum(maximum, part.max(axis=1, keepdims=True))
        exponents = [
            jnp.where(ok, jnp.exp(part - maximum), 0.0) for part, ok in zip(scores, allowed)
        ]
        denominator = exponents[0].sum(axis=1, keepdims=True)
        for part in exponents[1:]:
            denominator = denominator + part.sum(axis=1, keepdims=True)
        total = None
        for j in range(count):
            weights = (exponents[j] / denominator).astype(jnp.bfloat16)
            term = jnp.dot(weights, value_refs[j][...], preferred_element_type=jnp.float32)
            total = term if total is None else total + term
        out_ref[...] = total.astype(out_ref.dtype)

    in_specs = [pl.BlockSpec((tile_rows, head_dim), lambda h: (0, head_base + h))]
    operands = [queries]
    for key_array, value_array, key_block, value_block in slots:
        in_specs.append(pl.BlockSpec((tile_rows, head_dim), lambda h, b=key_block: (0, b + h)))
        in_specs.append(pl.BlockSpec((tile_rows, head_dim), lambda h, b=value_block: (0, b + h)))
        operands += [key_array, value_array]
    in_specs.append(pl.BlockSpec((1, count, tile_rows), lambda h: (h, 0, 0)))
    operands.append(usable.astype(jnp.int32))
    return pl.pallas_call(
        kernel,
        grid=(group_heads,),
        in_specs=in_specs,
        out_specs=pl.BlockSpec((tile_rows, head_dim), lambda h: (0, h)),
        out_shape=jax.ShapeDtypeStruct((tile_rows, group_heads * head_dim), queries.dtype),
    )(*operands)


def vertical_parts(devices, grid_rows):
    if grid_rows == 1:
        return []
    down = [(i, i + TW) for i in range(devices - TW)]
    up = [(i + TW, i) for i in range(devices - TW)]
    if grid_rows == 2:
        return [down + up]
    return [down, up]


def on_device(queries, keys, values, tile_lengths, head_windows, out_weight, gate):
    devices = lax.axis_size("seq")
    grid_rows = devices // TW
    tile_rows = queries.shape[0]
    feat_width = queries.shape[1]
    head_count = head_windows.shape[0]
    head_dim = feat_width // head_count
    score_scale = 1.0 / math.sqrt(head_dim)
    groups = GROUPS if head_count % GROUPS == 0 else 1
    group_heads = head_count // groups
    group_width = group_heads * head_dim

    to_right = [(i, i + 1) for i in range(devices) if i % TW < TW - 1]
    to_left = [(i + 1, i) for i in range(devices) if i % TW < TW - 1]
    sideways = lambda x: (lax.ppermute(x, "seq", to_right), lax.ppermute(x, "seq", to_left))

    weight_all = lax.all_gather(out_weight, "seq", axis=0, tiled=True)
    verticals = vertical_parts(devices, grid_rows)
    vert_lens = [lax.ppermute(tile_lengths, "seq", pairs) for pairs in verticals]
    column_lens = jnp.concatenate([tile_lengths] + vert_lens)
    left_lens, right_lens = sideways(column_lens)
    (left_k, left_v), (right_k, right_v) = sideways((keys, values))

    positions = jnp.arange(tile_rows, dtype=jnp.int32)
    query_real = positions < tile_lengths[0]
    rows = [0] + [1] * len(verticals)
    far_rows = jnp.array(rows * 3, jnp.int32)
    far_cols = jnp.array([0] * len(rows) + [1] * (2 * len(rows)), jnp.int32)
    length_stack = jnp.concatenate([column_lens, left_lens, right_lens])
    key_real = positions[None, :] < length_stack[:, None]

    def chunk(x, g):
        return lax.slice_in_dim(x, g * group_width, (g + 1) * group_width, axis=1)

    outputs = []
    previous = None
    for g in range(groups):
        own = jnp.concatenate([chunk(keys, g), chunk(values, g)], axis=1)
        if previous is not None:
            own, _ = lax.optimization_barrier((own, previous))
        got = [lax.ppermute(own, "seq", pairs) for pairs in verticals]
        if got:
            previous = got[-1]
        forwarded = [sideways(item) for item in got]
        base = g * group_heads
        slots = [(keys, values, base, base)]
        slots += [(item, item, 0, group_heads) for item in got]
        slots += [(left_k, left_v, base, base)]
        slots += [(item[0], item[0], 0, group_heads) for item in forwarded]
        slots += [(right_k, right_v, base, base)]
        slots += [(item[1], item[1], 0, group_heads) for item in forwarded]
        reach = lax.slice_in_dim(head_windows, base, base + group_heads, axis=0)
        window = (far_rows[None, :] <= reach[:, 0:1]) & (far_cols[None, :] <= reach[:, 1:2])
        usable = key_real[None, :, :] & window[:, :, None]
        attended = group_attention(queries, slots, usable, base, group_heads, head_dim, score_scale)
        outputs.append(jnp.where(query_real[:, None], attended, 0))

    attended_all = jnp.concatenate(outputs, axis=1)
    projected = jnp.dot(attended_all, weight_all, preferred_element_type=jnp.float32)
    return (projected * gate[None, :]).astype(jnp.bfloat16)


def solution(mesh):
    placed = (
        P(("groups", "seq"), None),
        P(("groups", "seq"), None),
        P(("groups", "seq"), None),
        P(("groups", "seq")),
        P(),
        P("seq", None),
        P("groups"),
    )

    return jax.shard_map(
        on_device, mesh=mesh, in_specs=placed, out_specs=P(("groups", "seq"), None), check_vma=False
    )
```

```python
import math

import jax
import jax.numpy as jnp
from jax import lax
from jax.experimental import pallas as pl
from jax.sharding import PartitionSpec as P


TW = 8
GROUPS = 4


def group_attention(queries, slots, usable, head_base, group_heads, head_dim, score_scale):
    tile_rows, _ = queries.shape
    count = len(slots)

    def kernel(*refs):
        query = refs[0][...]
        key_refs = refs[1:1 + 2 * count:2]
        value_refs = refs[2:2 + 2 * count:2]
        mask_ref = refs[1 + 2 * count]
        out_ref = refs[-1]
        scores = []
        allowed = []
        for j in range(count):
            part = lax.dot_general(
                query, key_refs[j][...], (((1,), (1,)), ((), ())),
                preferred_element_type=jnp.float32,
            ) * score_scale
            ok = mask_ref[0, j:j + 1, :] != 0
            scores.append(jnp.where(ok, part, -1e30))
            allowed.append(ok)
        maximum = scores[0].max(axis=1, keepdims=True)
        for part in scores[1:]:
            maximum = jnp.maximum(maximum, part.max(axis=1, keepdims=True))
        exponents = [
            jnp.where(ok, jnp.exp(part - maximum), 0.0) for part, ok in zip(scores, allowed)
        ]
        denominator = exponents[0].sum(axis=1, keepdims=True)
        for part in exponents[1:]:
            denominator = denominator + part.sum(axis=1, keepdims=True)
        total = None
        for j in range(count):
            weights = (exponents[j] / denominator).astype(jnp.bfloat16)
            term = jnp.dot(weights, value_refs[j][...], preferred_element_type=jnp.float32)
            total = term if total is None else total + term
        out_ref[...] = total.astype(out_ref.dtype)

    in_specs = [pl.BlockSpec((tile_rows, head_dim), lambda h: (0, head_base + h))]
    operands = [queries]
    for key_array, value_array, key_block, value_block in slots:
        in_specs.append(pl.BlockSpec((tile_rows, head_dim), lambda h, b=key_block: (0, b + h)))
        in_specs.append(pl.BlockSpec((tile_rows, head_dim), lambda h, b=value_block: (0, b + h)))
        operands += [key_array, value_array]
    in_specs.append(pl.BlockSpec((1, count, tile_rows), lambda h: (h, 0, 0)))
    operands.append(usable.astype(jnp.int32))
    return pl.pallas_call(
        kernel,
        grid=(group_heads,),
        in_specs=in_specs,
        out_specs=pl.BlockSpec((tile_rows, head_dim), lambda h: (0, h)),
        out_shape=jax.ShapeDtypeStruct((tile_rows, group_heads * head_dim), queries.dtype),
    )(*operands)


def vertical_parts(devices, grid_rows):
    if grid_rows == 1:
        return []
    down = [(i, i + TW) for i in range(devices - TW)]
    up = [(i + TW, i) for i in range(devices - TW)]
    if grid_rows == 2:
        return [down + up]
    return [down, up]


def on_device(queries, keys, values, tile_lengths, head_windows, out_weight, gate):
    devices = lax.axis_size("seq")
    grid_rows = devices // TW
    tile_rows = queries.shape[0]
    feat_width = queries.shape[1]
    head_count = head_windows.shape[0]
    head_dim = feat_width // head_count
    score_scale = 1.0 / math.sqrt(head_dim)
    groups = GROUPS if head_count % GROUPS == 0 else 1
    group_heads = head_count // groups
    group_width = group_heads * head_dim

    to_right = [(i, i + 1) for i in range(devices) if i % TW < TW - 1]
    to_left = [(i + 1, i) for i in range(devices) if i % TW < TW - 1]
    sideways = lambda x: (lax.ppermute(x, "seq", to_right), lax.ppermute(x, "seq", to_left))

    verticals = vertical_parts(devices, grid_rows)
    vertical_sources = []
    for pairs in verticals:
        table = [-1] * devices
        for s, r in pairs:
            table[r] = s
        vertical_sources.append(table)
    column_tables = [list(range(devices))] + vertical_sources
    left_tables = [[t[r - 1] if r % TW > 0 else -1 for r in range(devices)] for t in column_tables]
    right_tables = [[t[r + 1] if r % TW < TW - 1 else -1 for r in range(devices)] for t in column_tables]
    tables = jnp.array(column_tables + left_tables + right_tables, jnp.int32)
    all_lens = lax.all_gather(tile_lengths, "seq", axis=0, tiled=True)
    slot_source = tables[:, lax.axis_index("seq")]
    length_stack = jnp.where(slot_source >= 0, all_lens[jnp.maximum(slot_source, 0)], 0)
    weight_part, _ = lax.optimization_barrier((out_weight, all_lens))
    weight_all = lax.all_gather(weight_part, "seq", axis=0, tiled=True)
    (left_k, left_v), (right_k, right_v) = sideways((keys, values))

    positions = jnp.arange(tile_rows, dtype=jnp.int32)
    query_real = positions < tile_lengths[0]
    rows = [0] + [1] * len(verticals)
    far_rows = jnp.array(rows * 3, jnp.int32)
    far_cols = jnp.array([0] * len(rows) + [1] * (2 * len(rows)), jnp.int32)
    key_real = positions[None, :] < length_stack[:, None]

    def chunk(x, g):
        return lax.slice_in_dim(x, g * group_width, (g + 1) * group_width, axis=1)

    outputs = []
    previous = None
    for g in range(groups):
        own = jnp.concatenate([chunk(keys, g), chunk(values, g)], axis=1)
        if previous is not None:
            own, _ = lax.optimization_barrier((own, previous))
        got = [lax.ppermute(own, "seq", pairs) for pairs in verticals]
        if got:
            previous = got[-1]
        forwarded = [sideways(item) for item in got]
        base = g * group_heads
        slots = [(keys, values, base, base)]
        slots += [(item, item, 0, group_heads) for item in got]
        slots += [(left_k, left_v, base, base)]
        slots += [(item[0], item[0], 0, group_heads) for item in forwarded]
        slots += [(right_k, right_v, base, base)]
        slots += [(item[1], item[1], 0, group_heads) for item in forwarded]
        reach = lax.slice_in_dim(head_windows, base, base + group_heads, axis=0)
        window = (far_rows[None, :] <= reach[:, 0:1]) & (far_cols[None, :] <= reach[:, 1:2])
        usable = key_real[None, :, :] & window[:, :, None]
        attended = group_attention(queries, slots, usable, base, group_heads, head_dim, score_scale)
        outputs.append(jnp.where(query_real[:, None], attended, 0))

    attended_all = jnp.concatenate(outputs, axis=1)
    projected = jnp.dot(attended_all, weight_all, preferred_element_type=jnp.float32)
    return (projected * gate[None, :]).astype(jnp.bfloat16)


def solution(mesh):
    placed = (
        P(("groups", "seq"), None),
        P(("groups", "seq"), None),
        P(("groups", "seq"), None),
        P(("groups", "seq")),
        P(),
        P("seq", None),
        P("groups"),
    )

    return jax.shard_map(
        on_device, mesh=mesh, in_specs=placed, out_specs=P(("groups", "seq"), None), check_vma=False
    )
```

```python
import math

import jax
import jax.numpy as jnp
from jax import lax
from jax.experimental import pallas as pl
from jax.sharding import PartitionSpec as P


TW = 8
GROUPS = 3


def group_attention(queries, slots, usable, head_base, group_heads, head_dim, score_scale):
    tile_rows, _ = queries.shape
    count = len(slots)

    def kernel(*refs):
        query = refs[0][...]
        key_refs = refs[1:1 + 2 * count:2]
        value_refs = refs[2:2 + 2 * count:2]
        mask_ref = refs[1 + 2 * count]
        out_ref = refs[-1]
        scores = []
        allowed = []
        for j in range(count):
            part = lax.dot_general(
                query, key_refs[j][...], (((1,), (1,)), ((), ())),
                preferred_element_type=jnp.float32,
            ) * score_scale
            ok = mask_ref[0, j:j + 1, :] != 0
            scores.append(jnp.where(ok, part, -1e30))
            allowed.append(ok)
        maximum = scores[0].max(axis=1, keepdims=True)
        for part in scores[1:]:
            maximum = jnp.maximum(maximum, part.max(axis=1, keepdims=True))
        exponents = [
            jnp.where(ok, jnp.exp(part - maximum), 0.0) for part, ok in zip(scores, allowed)
        ]
        denominator = exponents[0].sum(axis=1, keepdims=True)
        for part in exponents[1:]:
            denominator = denominator + part.sum(axis=1, keepdims=True)
        total = None
        for j in range(count):
            weights = (exponents[j] / denominator).astype(jnp.bfloat16)
            term = jnp.dot(weights, value_refs[j][...], preferred_element_type=jnp.float32)
            total = term if total is None else total + term
        out_ref[...] = total.astype(out_ref.dtype)

    in_specs = [pl.BlockSpec((tile_rows, head_dim), lambda h: (0, head_base + h))]
    operands = [queries]
    for key_array, value_array, key_block, value_block in slots:
        in_specs.append(pl.BlockSpec((tile_rows, head_dim), lambda h, b=key_block: (0, b + h)))
        in_specs.append(pl.BlockSpec((tile_rows, head_dim), lambda h, b=value_block: (0, b + h)))
        operands += [key_array, value_array]
    in_specs.append(pl.BlockSpec((1, count, tile_rows), lambda h: (h, 0, 0)))
    operands.append(usable.astype(jnp.int32))
    return pl.pallas_call(
        kernel,
        grid=(group_heads,),
        in_specs=in_specs,
        out_specs=pl.BlockSpec((tile_rows, head_dim), lambda h: (0, h)),
        out_shape=jax.ShapeDtypeStruct((tile_rows, group_heads * head_dim), queries.dtype),
    )(*operands)


def vertical_parts(devices, grid_rows):
    if grid_rows == 1:
        return []
    down = [(i, i + TW) for i in range(devices - TW)]
    up = [(i + TW, i) for i in range(devices - TW)]
    if grid_rows == 2:
        return [down + up]
    return [down, up]


def on_device(queries, keys, values, tile_lengths, head_windows, out_weight, gate):
    devices = lax.axis_size("seq")
    grid_rows = devices // TW
    tile_rows = queries.shape[0]
    feat_width = queries.shape[1]
    head_count = head_windows.shape[0]
    head_dim = feat_width // head_count
    score_scale = 1.0 / math.sqrt(head_dim)
    groups = GROUPS if head_count % GROUPS == 0 else 1
    group_heads = head_count // groups
    group_width = group_heads * head_dim

    to_right = [(i, i + 1) for i in range(devices) if i % TW < TW - 1]
    to_left = [(i + 1, i) for i in range(devices) if i % TW < TW - 1]
    sideways = lambda x: (lax.ppermute(x, "seq", to_right), lax.ppermute(x, "seq", to_left))

    verticals = vertical_parts(devices, grid_rows)
    left_of = lambda pairs: [(s, r + 1) for s, r in pairs if r % TW < TW - 1]
    right_of = lambda pairs: [(s, r - 1) for s, r in pairs if r % TW > 0]
    fetch = lambda pairs: lax.ppermute(tile_lengths, "seq", pairs)
    vert_lens = [fetch(pairs) for pairs in verticals]
    column_lens = jnp.concatenate([tile_lengths] + vert_lens)
    left_lens = jnp.concatenate([fetch(to_right)] + [fetch(left_of(p)) for p in verticals])
    right_lens = jnp.concatenate([fetch(to_left)] + [fetch(right_of(p)) for p in verticals])
    (left_k, left_v), (right_k, right_v) = sideways((keys, values))

    positions = jnp.arange(tile_rows, dtype=jnp.int32)
    query_real = positions < tile_lengths[0]
    rows = [0] + [1] * len(verticals)
    far_rows = jnp.array(rows * 3, jnp.int32)
    far_cols = jnp.array([0] * len(rows) + [1] * (2 * len(rows)), jnp.int32)
    length_stack = jnp.concatenate([column_lens, left_lens, right_lens])
    key_real = positions[None, :] < length_stack[:, None]

    def chunk(x, g):
        return lax.slice_in_dim(x, g * group_width, (g + 1) * group_width, axis=1)

    outputs = []
    previous = None
    for g in range(groups):
        own = jnp.concatenate([chunk(keys, g), chunk(values, g)], axis=1)
        if previous is not None:
            own, _ = lax.optimization_barrier((own, previous))
        got = [lax.ppermute(own, "seq", pairs) for pairs in verticals]
        if got:
            previous = got[-1]
        if g == 0:
            weight_part, _ = lax.optimization_barrier((out_weight, got[-1] if got else own))
            weight_all = lax.all_gather(weight_part, "seq", axis=0, tiled=True)
        forwarded = [sideways(item) for item in got]
        base = g * group_heads
        slots = [(keys, values, base, base)]
        slots += [(item, item, 0, group_heads) for item in got]
        slots += [(left_k, left_v, base, base)]
        slots += [(item[0], item[0], 0, group_heads) for item in forwarded]
        slots += [(right_k, right_v, base, base)]
        slots += [(item[1], item[1], 0, group_heads) for item in forwarded]
        reach = lax.slice_in_dim(head_windows, base, base + group_heads, axis=0)
        window = (far_rows[None, :] <= reach[:, 0:1]) & (far_cols[None, :] <= reach[:, 1:2])
        usable = key_real[None, :, :] & window[:, :, None]
        attended = group_attention(queries, slots, usable, base, group_heads, head_dim, score_scale)
        outputs.append(jnp.where(query_real[:, None], attended, 0))

    attended_all = jnp.concatenate(outputs, axis=1)
    projected = jnp.dot(attended_all, weight_all, preferred_element_type=jnp.float32)
    return (projected * gate[None, :]).astype(jnp.bfloat16)


def solution(mesh):
    placed = (
        P(("groups", "seq"), None),
        P(("groups", "seq"), None),
        P(("groups", "seq"), None),
        P(("groups", "seq")),
        P(),
        P("seq", None),
        P("groups"),
    )

    return jax.shard_map(
        on_device, mesh=mesh, in_specs=placed, out_specs=P(("groups", "seq"), None), check_vma=False
    )
```

```python
import math

import jax
import jax.numpy as jnp
from jax import lax
from jax.experimental import pallas as pl
from jax.sharding import PartitionSpec as P


TW = 8
GROUPS = 3


def group_attention(queries, slots, usable, head_base, group_heads, head_dim, score_scale):
    tile_rows, _ = queries.shape
    count = len(slots)

    def kernel(*refs):
        query = refs[0][...]
        key_refs = refs[1:1 + 2 * count:2]
        value_refs = refs[2:2 + 2 * count:2]
        mask_ref = refs[1 + 2 * count]
        out_ref = refs[-1]
        scores = []
        allowed = []
        for j in range(count):
            part = lax.dot_general(
                query, key_refs[j][...], (((1,), (1,)), ((), ())),
                preferred_element_type=jnp.float32,
            ) * score_scale
            ok = mask_ref[0, j:j + 1, :] != 0
            scores.append(jnp.where(ok, part, -1e30))
            allowed.append(ok)
        maximum = scores[0].max(axis=1, keepdims=True)
        for part in scores[1:]:
            maximum = jnp.maximum(maximum, part.max(axis=1, keepdims=True))
        exponents = [
            jnp.where(ok, jnp.exp(part - maximum), 0.0) for part, ok in zip(scores, allowed)
        ]
        denominator = exponents[0].sum(axis=1, keepdims=True)
        for part in exponents[1:]:
            denominator = denominator + part.sum(axis=1, keepdims=True)
        total = None
        for j in range(count):
            weights = (exponents[j] / denominator).astype(jnp.bfloat16)
            term = jnp.dot(weights, value_refs[j][...], preferred_element_type=jnp.float32)
            total = term if total is None else total + term
        out_ref[...] = total.astype(out_ref.dtype)

    in_specs = [pl.BlockSpec((tile_rows, head_dim), lambda h: (0, head_base + h))]
    operands = [queries]
    for key_array, value_array, key_block, value_block in slots:
        in_specs.append(pl.BlockSpec((tile_rows, head_dim), lambda h, b=key_block: (0, b + h)))
        in_specs.append(pl.BlockSpec((tile_rows, head_dim), lambda h, b=value_block: (0, b + h)))
        operands += [key_array, value_array]
    in_specs.append(pl.BlockSpec((1, count, tile_rows), lambda h: (h, 0, 0)))
    operands.append(usable.astype(jnp.int32))
    return pl.pallas_call(
        kernel,
        grid=(group_heads,),
        in_specs=in_specs,
        out_specs=pl.BlockSpec((tile_rows, head_dim), lambda h: (0, h)),
        out_shape=jax.ShapeDtypeStruct((tile_rows, group_heads * head_dim), queries.dtype),
    )(*operands)


def vertical_parts(devices, grid_rows):
    if grid_rows == 1:
        return []
    down = [(i, i + TW) for i in range(devices - TW)]
    up = [(i + TW, i) for i in range(devices - TW)]
    if grid_rows == 2:
        return [down + up]
    return [down, up]


def on_device(queries, keys, values, tile_lengths, head_windows, out_weight, gate):
    devices = lax.axis_size("seq")
    grid_rows = devices // TW
    tile_rows = queries.shape[0]
    feat_width = queries.shape[1]
    head_count = head_windows.shape[0]
    head_dim = feat_width // head_count
    score_scale = 1.0 / math.sqrt(head_dim)
    groups = GROUPS if head_count % GROUPS == 0 else 1
    group_heads = head_count // groups
    group_width = group_heads * head_dim

    to_right = [(i, i + 1) for i in range(devices) if i % TW < TW - 1]
    to_left = [(i + 1, i) for i in range(devices) if i % TW < TW - 1]
    sideways = lambda x: (lax.ppermute(x, "seq", to_right), lax.ppermute(x, "seq", to_left))

    column_groups = [[c + TW * r for r in range(grid_rows)] for c in range(TW)]
    row_groups = [[c + TW * r for c in range(TW)] for r in range(grid_rows)]
    weight_col = lax.all_gather(out_weight, "seq", axis=0, axis_index_groups=column_groups)
    verticals = vertical_parts(devices, grid_rows)
    left_of = lambda pairs: [(s, r + 1) for s, r in pairs if r % TW < TW - 1]
    right_of = lambda pairs: [(s, r - 1) for s, r in pairs if r % TW > 0]
    fetch = lambda pairs: lax.ppermute(tile_lengths, "seq", pairs)
    vert_lens = [fetch(pairs) for pairs in verticals]
    column_lens = jnp.concatenate([tile_lengths] + vert_lens)
    left_lens = jnp.concatenate([fetch(to_right)] + [fetch(left_of(p)) for p in verticals])
    right_lens = jnp.concatenate([fetch(to_left)] + [fetch(right_of(p)) for p in verticals])
    (left_k, left_v), (right_k, right_v) = sideways((keys, values))

    positions = jnp.arange(tile_rows, dtype=jnp.int32)
    query_real = positions < tile_lengths[0]
    rows = [0] + [1] * len(verticals)
    far_rows = jnp.array(rows * 3, jnp.int32)
    far_cols = jnp.array([0] * len(rows) + [1] * (2 * len(rows)), jnp.int32)
    length_stack = jnp.concatenate([column_lens, left_lens, right_lens])
    key_real = positions[None, :] < length_stack[:, None]

    def chunk(x, g):
        return lax.slice_in_dim(x, g * group_width, (g + 1) * group_width, axis=1)

    outputs = []
    previous = None
    for g in range(groups):
        own = jnp.concatenate([chunk(keys, g), chunk(values, g)], axis=1)
        if previous is not None:
            own, _ = lax.optimization_barrier((own, previous))
        got = [lax.ppermute(own, "seq", pairs) for pairs in verticals]
        if got:
            previous = got[-1]
        if g == 0:
            weight_col, _ = lax.optimization_barrier((weight_col, got[-1] if got else own))
            weight_grid = lax.all_gather(weight_col, "seq", axis=0, axis_index_groups=row_groups)
            weight_all = jnp.swapaxes(weight_grid, 0, 1).reshape(-1, out_weight.shape[1])
        forwarded = [sideways(item) for item in got]
        base = g * group_heads
        slots = [(keys, values, base, base)]
        slots += [(item, item, 0, group_heads) for item in got]
        slots += [(left_k, left_v, base, base)]
        slots += [(item[0], item[0], 0, group_heads) for item in forwarded]
        slots += [(right_k, right_v, base, base)]
        slots += [(item[1], item[1], 0, group_heads) for item in forwarded]
        reach = lax.slice_in_dim(head_windows, base, base + group_heads, axis=0)
        window = (far_rows[None, :] <= reach[:, 0:1]) & (far_cols[None, :] <= reach[:, 1:2])
        usable = key_real[None, :, :] & window[:, :, None]
        attended = group_attention(queries, slots, usable, base, group_heads, head_dim, score_scale)
        outputs.append(jnp.where(query_real[:, None], attended, 0))

    attended_all = jnp.concatenate(outputs, axis=1)
    projected = jnp.dot(attended_all, weight_all, preferred_element_type=jnp.float32)
    return (projected * gate[None, :]).astype(jnp.bfloat16)


def solution(mesh):
    placed = (
        P(("groups", "seq"), None),
        P(("groups", "seq"), None),
        P(("groups", "seq"), None),
        P(("groups", "seq")),
        P(),
        P("seq", None),
        P("groups"),
    )

    return jax.shard_map(
        on_device, mesh=mesh, in_specs=placed, out_specs=P(("groups", "seq"), None), check_vma=False
    )
```

```python
import math

import jax
import jax.numpy as jnp
from jax import lax
from jax.experimental import pallas as pl
from jax.sharding import PartitionSpec as P


TW = 8
GROUPS = 2


def group_attention(queries, slots, usable, head_base, group_heads, head_dim, score_scale):
    tile_rows, _ = queries.shape
    count = len(slots)

    def kernel(*refs):
        query = refs[0][...]
        key_refs = refs[1:1 + 2 * count:2]
        value_refs = refs[2:2 + 2 * count:2]
        mask_ref = refs[1 + 2 * count]
        out_ref = refs[-1]
        scores = []
        allowed = []
        for j in range(count):
            part = lax.dot_general(
                query, key_refs[j][...], (((1,), (1,)), ((), ())),
                preferred_element_type=jnp.float32,
            ) * score_scale
            ok = mask_ref[0, j:j + 1, :] != 0
            scores.append(jnp.where(ok, part, -1e30))
            allowed.append(ok)
        maximum = scores[0].max(axis=1, keepdims=True)
        for part in scores[1:]:
            maximum = jnp.maximum(maximum, part.max(axis=1, keepdims=True))
        exponents = [
            jnp.where(ok, jnp.exp(part - maximum), 0.0) for part, ok in zip(scores, allowed)
        ]
        denominator = exponents[0].sum(axis=1, keepdims=True)
        for part in exponents[1:]:
            denominator = denominator + part.sum(axis=1, keepdims=True)
        total = None
        for j in range(count):
            weights = (exponents[j] / denominator).astype(jnp.bfloat16)
            term = jnp.dot(weights, value_refs[j][...], preferred_element_type=jnp.float32)
            total = term if total is None else total + term
        out_ref[...] = total.astype(out_ref.dtype)

    in_specs = [pl.BlockSpec((tile_rows, head_dim), lambda h: (0, head_base + h))]
    operands = [queries]
    for key_array, value_array, key_block, value_block in slots:
        in_specs.append(pl.BlockSpec((tile_rows, head_dim), lambda h, b=key_block: (0, b + h)))
        in_specs.append(pl.BlockSpec((tile_rows, head_dim), lambda h, b=value_block: (0, b + h)))
        operands += [key_array, value_array]
    in_specs.append(pl.BlockSpec((1, count, tile_rows), lambda h: (h, 0, 0)))
    operands.append(usable.astype(jnp.int32))
    return pl.pallas_call(
        kernel,
        grid=(group_heads,),
        in_specs=in_specs,
        out_specs=pl.BlockSpec((tile_rows, head_dim), lambda h: (0, h)),
        out_shape=jax.ShapeDtypeStruct((tile_rows, group_heads * head_dim), queries.dtype),
    )(*operands)


def vertical_parts(devices, grid_rows):
    if grid_rows == 1:
        return []
    down = [(i, i + TW) for i in range(devices - TW)]
    up = [(i + TW, i) for i in range(devices - TW)]
    if grid_rows == 2:
        return [down + up]
    return [down, up]


def on_device(queries, keys, values, tile_lengths, head_windows, out_weight, gate):
    devices = lax.axis_size("seq")
    grid_rows = devices // TW
    tile_rows = queries.shape[0]
    feat_width = queries.shape[1]
    head_count = head_windows.shape[0]
    head_dim = feat_width // head_count
    score_scale = 1.0 / math.sqrt(head_dim)
    groups = GROUPS if head_count % GROUPS == 0 else 1
    group_heads = head_count // groups
    group_width = group_heads * head_dim

    to_right = [(i, i + 1) for i in range(devices) if i % TW < TW - 1]
    to_left = [(i + 1, i) for i in range(devices) if i % TW < TW - 1]
    sideways = lambda x: (lax.ppermute(x, "seq", to_right), lax.ppermute(x, "seq", to_left))

    weight_all = lax.all_gather(out_weight, "seq", axis=0, tiled=True)
    verticals = vertical_parts(devices, grid_rows)
    left_of = lambda pairs: [(s, r + 1) for s, r in pairs if r % TW < TW - 1]
    right_of = lambda pairs: [(s, r - 1) for s, r in pairs if r % TW > 0]
    fetch = lambda pairs: lax.ppermute(tile_lengths, "seq", pairs)
    vert_lens = [fetch(pairs) for pairs in verticals]
    column_lens = jnp.concatenate([tile_lengths] + vert_lens)
    left_lens = jnp.concatenate([fetch(to_right)] + [fetch(left_of(p)) for p in verticals])
    right_lens = jnp.concatenate([fetch(to_left)] + [fetch(right_of(p)) for p in verticals])
    (left_k, left_v), (right_k, right_v) = sideways((keys, values))

    positions = jnp.arange(tile_rows, dtype=jnp.int32)
    query_real = positions < tile_lengths[0]
    rows = [0] + [1] * len(verticals)
    far_rows = jnp.array(rows * 3, jnp.int32)
    far_cols = jnp.array([0] * len(rows) + [1] * (2 * len(rows)), jnp.int32)
    length_stack = jnp.concatenate([column_lens, left_lens, right_lens])
    key_real = positions[None, :] < length_stack[:, None]

    def chunk(x, g):
        return lax.slice_in_dim(x, g * group_width, (g + 1) * group_width, axis=1)

    outputs = []
    previous = None
    for g in range(groups):
        own = jnp.concatenate([chunk(keys, g), chunk(values, g)], axis=1)
        if previous is not None:
            own, _ = lax.optimization_barrier((own, previous))
        got = [lax.ppermute(own, "seq", pairs) for pairs in verticals]
        if got:
            previous = got[-1]
        forwarded = [sideways(item) for item in got]
        base = g * group_heads
        slots = [(keys, values, base, base)]
        slots += [(item, item, 0, group_heads) for item in got]
        slots += [(left_k, left_v, base, base)]
        slots += [(item[0], item[0], 0, group_heads) for item in forwarded]
        slots += [(right_k, right_v, base, base)]
        slots += [(item[1], item[1], 0, group_heads) for item in forwarded]
        reach = lax.slice_in_dim(head_windows, base, base + group_heads, axis=0)
        window = (far_rows[None, :] <= reach[:, 0:1]) & (far_cols[None, :] <= reach[:, 1:2])
        usable = key_real[None, :, :] & window[:, :, None]
        attended = group_attention(queries, slots, usable, base, group_heads, head_dim, score_scale)
        outputs.append(jnp.where(query_real[:, None], attended, 0))

    attended_all = jnp.concatenate(outputs, axis=1)
    projected = jnp.dot(attended_all, weight_all, preferred_element_type=jnp.float32)
    return (projected * gate[None, :]).astype(jnp.bfloat16)


def solution(mesh):
    placed = (
        P(("groups", "seq"), None),
        P(("groups", "seq"), None),
        P(("groups", "seq"), None),
        P(("groups", "seq")),
        P(),
        P("seq", None),
        P("groups"),
    )

    return jax.shard_map(
        on_device, mesh=mesh, in_specs=placed, out_specs=P(("groups", "seq"), None), check_vma=False
    )
```

```python
import math

import jax
import jax.numpy as jnp
from jax import lax
from jax.experimental import pallas as pl
from jax.sharding import PartitionSpec as P


TW = 8
GROUPS = 3


def group_attention(queries, slots, usable, head_base, group_heads, head_dim, score_scale):
    tile_rows, _ = queries.shape
    count = len(slots)

    def kernel(*refs):
        query = refs[0][...]
        key_refs = refs[1:1 + 2 * count:2]
        value_refs = refs[2:2 + 2 * count:2]
        mask_ref = refs[1 + 2 * count]
        out_ref = refs[-1]
        scores = []
        allowed = []
        for j in range(count):
            part = lax.dot_general(
                query, key_refs[j][...], (((1,), (1,)), ((), ())),
                preferred_element_type=jnp.float32,
            ) * score_scale
            ok = mask_ref[0, j:j + 1, :] != 0
            scores.append(jnp.where(ok, part, -1e30))
            allowed.append(ok)
        maximum = scores[0].max(axis=1, keepdims=True)
        for part in scores[1:]:
            maximum = jnp.maximum(maximum, part.max(axis=1, keepdims=True))
        exponents = [
            jnp.where(ok, jnp.exp(part - maximum), 0.0) for part, ok in zip(scores, allowed)
        ]
        denominator = exponents[0].sum(axis=1, keepdims=True)
        for part in exponents[1:]:
            denominator = denominator + part.sum(axis=1, keepdims=True)
        total = None
        for j in range(count):
            weights = (exponents[j] / denominator).astype(jnp.bfloat16)
            term = jnp.dot(weights, value_refs[j][...], preferred_element_type=jnp.float32)
            total = term if total is None else total + term
        out_ref[...] = total.astype(out_ref.dtype)

    in_specs = [pl.BlockSpec((tile_rows, head_dim), lambda h: (0, head_base + h))]
    operands = [queries]
    for key_array, value_array, key_block, value_block in slots:
        in_specs.append(pl.BlockSpec((tile_rows, head_dim), lambda h, b=key_block: (0, b + h)))
        in_specs.append(pl.BlockSpec((tile_rows, head_dim), lambda h, b=value_block: (0, b + h)))
        operands += [key_array, value_array]
    in_specs.append(pl.BlockSpec((1, count, tile_rows), lambda h: (h, 0, 0)))
    operands.append(usable.astype(jnp.int32))
    return pl.pallas_call(
        kernel,
        grid=(group_heads,),
        in_specs=in_specs,
        out_specs=pl.BlockSpec((tile_rows, head_dim), lambda h: (0, h)),
        out_shape=jax.ShapeDtypeStruct((tile_rows, group_heads * head_dim), queries.dtype),
    )(*operands)


def vertical_parts(devices, grid_rows):
    if grid_rows == 1:
        return []
    down = [(i, i + TW) for i in range(devices - TW)]
    up = [(i + TW, i) for i in range(devices - TW)]
    if grid_rows == 2:
        return [down + up]
    return [down, up]


def on_device(queries, keys, values, tile_lengths, head_windows, out_weight, gate):
    devices = lax.axis_size("seq")
    grid_rows = devices // TW
    tile_rows = queries.shape[0]
    feat_width = queries.shape[1]
    head_count = head_windows.shape[0]
    head_dim = feat_width // head_count
    score_scale = 1.0 / math.sqrt(head_dim)
    groups = GROUPS if head_count % GROUPS == 0 else 1
    group_heads = head_count // groups
    group_width = group_heads * head_dim

    to_right = [(i, i + 1) for i in range(devices) if i % TW < TW - 1]
    to_left = [(i + 1, i) for i in range(devices) if i % TW < TW - 1]
    sideways = lambda x: (lax.ppermute(x, "seq", to_right), lax.ppermute(x, "seq", to_left))

    parity_groups = [list(range(p, devices, 2)) for p in range(2)]
    weight_same = lax.all_gather(
        out_weight, "seq", axis=0, tiled=True, axis_index_groups=parity_groups
    )
    verticals = vertical_parts(devices, grid_rows)
    left_of = lambda pairs: [(s, r + 1) for s, r in pairs if r % TW < TW - 1]
    right_of = lambda pairs: [(s, r - 1) for s, r in pairs if r % TW > 0]
    fetch = lambda pairs: lax.ppermute(tile_lengths, "seq", pairs)
    vert_lens = [fetch(pairs) for pairs in verticals]
    column_lens = jnp.concatenate([tile_lengths] + vert_lens)
    left_lens = jnp.concatenate([fetch(to_right)] + [fetch(left_of(p)) for p in verticals])
    right_lens = jnp.concatenate([fetch(to_left)] + [fetch(right_of(p)) for p in verticals])
    (left_k, left_v), (right_k, right_v) = sideways((keys, values))

    positions = jnp.arange(tile_rows, dtype=jnp.int32)
    query_real = positions < tile_lengths[0]
    rows = [0] + [1] * len(verticals)
    far_rows = jnp.array(rows * 3, jnp.int32)
    far_cols = jnp.array([0] * len(rows) + [1] * (2 * len(rows)), jnp.int32)
    length_stack = jnp.concatenate([column_lens, left_lens, right_lens])
    key_real = positions[None, :] < length_stack[:, None]

    def chunk(x, g):
        return lax.slice_in_dim(x, g * group_width, (g + 1) * group_width, axis=1)

    outputs = []
    previous = None
    for g in range(groups):
        own = jnp.concatenate([chunk(keys, g), chunk(values, g)], axis=1)
        if previous is not None:
            own, _ = lax.optimization_barrier((own, previous))
        got = [lax.ppermute(own, "seq", pairs) for pairs in verticals]
        if got:
            previous = got[-1]
        if g == min(1, groups - 1):
            weight_same, _ = lax.optimization_barrier((weight_same, got[-1] if got else own))
            weight_other = lax.ppermute(weight_same, "seq", [(i, i ^ 1) for i in range(devices)])
        forwarded = [sideways(item) for item in got]
        base = g * group_heads
        slots = [(keys, values, base, base)]
        slots += [(item, item, 0, group_heads) for item in got]
        slots += [(left_k, left_v, base, base)]
        slots += [(item[0], item[0], 0, group_heads) for item in forwarded]
        slots += [(right_k, right_v, base, base)]
        slots += [(item[1], item[1], 0, group_heads) for item in forwarded]
        reach = lax.slice_in_dim(head_windows, base, base + group_heads, axis=0)
        window = (far_rows[None, :] <= reach[:, 0:1]) & (far_cols[None, :] <= reach[:, 1:2])
        usable = key_real[None, :, :] & window[:, :, None]
        attended = group_attention(queries, slots, usable, base, group_heads, head_dim, score_scale)
        outputs.append(jnp.where(query_real[:, None], attended, 0))

    attended_all = jnp.concatenate(outputs, axis=1)
    shard_rows = out_weight.shape[0]
    split = attended_all.reshape(tile_rows, devices // 2, 2, shard_rows)
    parity = lax.axis_index("seq") % 2
    same = jnp.where(parity == 0, split[:, :, 0], split[:, :, 1]).reshape(tile_rows, -1)
    other = jnp.where(parity == 0, split[:, :, 1], split[:, :, 0]).reshape(tile_rows, -1)
    projected = jnp.dot(same, weight_same, preferred_element_type=jnp.float32) + jnp.dot(
        other, weight_other, preferred_element_type=jnp.float32
    )
    return (projected * gate[None, :]).astype(jnp.bfloat16)


def solution(mesh):
    placed = (
        P(("groups", "seq"), None),
        P(("groups", "seq"), None),
        P(("groups", "seq"), None),
        P(("groups", "seq")),
        P(),
        P("seq", None),
        P("groups"),
    )

    return jax.shard_map(
        on_device, mesh=mesh, in_specs=placed, out_specs=P(("groups", "seq"), None), check_vma=False
    )
```

```python
import math

import jax
import jax.numpy as jnp
from jax import lax
from jax.experimental import pallas as pl
from jax.sharding import PartitionSpec as P


TW = 8
GROUPS = 3


def group_attention(queries, slots, usable, head_base, group_heads, head_dim, score_scale):
    tile_rows, _ = queries.shape
    count = len(slots)

    def kernel(*refs):
        query = refs[0][...]
        key_refs = refs[1:1 + 2 * count:2]
        value_refs = refs[2:2 + 2 * count:2]
        mask_ref = refs[1 + 2 * count]
        out_ref = refs[-1]
        scores = []
        allowed = []
        for j in range(count):
            part = lax.dot_general(
                query, key_refs[j][...], (((1,), (1,)), ((), ())),
                preferred_element_type=jnp.float32,
            ) * score_scale
            ok = mask_ref[0, j:j + 1, :] != 0
            scores.append(jnp.where(ok, part, -1e30))
            allowed.append(ok)
        maximum = scores[0].max(axis=1, keepdims=True)
        for part in scores[1:]:
            maximum = jnp.maximum(maximum, part.max(axis=1, keepdims=True))
        exponents = [
            jnp.where(ok, jnp.exp(part - maximum), 0.0) for part, ok in zip(scores, allowed)
        ]
        denominator = exponents[0].sum(axis=1, keepdims=True)
        for part in exponents[1:]:
            denominator = denominator + part.sum(axis=1, keepdims=True)
        total = None
        for j in range(count):
            weights = (exponents[j] / denominator).astype(jnp.bfloat16)
            term = jnp.dot(weights, value_refs[j][...], preferred_element_type=jnp.float32)
            total = term if total is None else total + term
        out_ref[...] = total.astype(out_ref.dtype)

    in_specs = [pl.BlockSpec((tile_rows, head_dim), lambda h: (0, head_base + h))]
    operands = [queries]
    for key_array, value_array, key_block, value_block in slots:
        in_specs.append(pl.BlockSpec((tile_rows, head_dim), lambda h, b=key_block: (0, b + h)))
        in_specs.append(pl.BlockSpec((tile_rows, head_dim), lambda h, b=value_block: (0, b + h)))
        operands += [key_array, value_array]
    in_specs.append(pl.BlockSpec((1, count, tile_rows), lambda h: (h, 0, 0)))
    operands.append(usable.astype(jnp.int32))
    return pl.pallas_call(
        kernel,
        grid=(group_heads,),
        in_specs=in_specs,
        out_specs=pl.BlockSpec((tile_rows, head_dim), lambda h: (0, h)),
        out_shape=jax.ShapeDtypeStruct((tile_rows, group_heads * head_dim), queries.dtype),
    )(*operands)


def vertical_parts(devices, grid_rows):
    if grid_rows == 1:
        return []
    down = [(i, i + TW) for i in range(devices - TW)]
    up = [(i + TW, i) for i in range(devices - TW)]
    if grid_rows == 2:
        return [down + up]
    return [down, up]


def on_device(queries, keys, values, tile_lengths, head_windows, out_weight, gate):
    devices = lax.axis_size("seq")
    grid_rows = devices // TW
    tile_rows = queries.shape[0]
    feat_width = queries.shape[1]
    head_count = head_windows.shape[0]
    head_dim = feat_width // head_count
    score_scale = 1.0 / math.sqrt(head_dim)
    groups = GROUPS if head_count % GROUPS == 0 else 1
    group_heads = head_count // groups
    group_width = group_heads * head_dim

    to_right = [(i, i + 1) for i in range(devices) if i % TW < TW - 1]
    to_left = [(i + 1, i) for i in range(devices) if i % TW < TW - 1]
    sideways = lambda x: (lax.ppermute(x, "seq", to_right), lax.ppermute(x, "seq", to_left))

    weight_all = lax.all_gather(out_weight, "seq", axis=0, tiled=True)
    verticals = vertical_parts(devices, grid_rows)
    left_of = lambda pairs: [(s, r + 1) for s, r in pairs if r % TW < TW - 1]
    right_of = lambda pairs: [(s, r - 1) for s, r in pairs if r % TW > 0]
    fetch = lambda pairs: lax.ppermute(tile_lengths, "seq", pairs)
    vert_lens = [fetch(pairs) for pairs in verticals]
    column_lens = jnp.concatenate([tile_lengths] + vert_lens)
    left_lens = jnp.concatenate([fetch(to_right)] + [fetch(left_of(p)) for p in verticals])
    right_lens = jnp.concatenate([fetch(to_left)] + [fetch(right_of(p)) for p in verticals])
    (left_k, left_v), (right_k, right_v) = sideways((keys, values))

    positions = jnp.arange(tile_rows, dtype=jnp.int32)
    query_real = positions < tile_lengths[0]
    rows = [0] + [1] * len(verticals)
    far_rows = jnp.array(rows * 3, jnp.int32)
    far_cols = jnp.array([0] * len(rows) + [1] * (2 * len(rows)), jnp.int32)
    length_stack = jnp.concatenate([column_lens, left_lens, right_lens])
    key_real = positions[None, :] < length_stack[:, None]

    def chunk(x, g):
        return lax.slice_in_dim(x, g * group_width, (g + 1) * group_width, axis=1)

    outputs = []
    previous = None
    for g in range(groups):
        own = jnp.concatenate([chunk(keys, g), chunk(values, g)], axis=1)
        if previous is not None:
            own, _ = lax.optimization_barrier((own, previous))
        got = [lax.ppermute(own, "seq", pairs) for pairs in verticals]
        if got:
            previous = got[-1]
        forwarded = [sideways(item) for item in got]
        base = g * group_heads
        slots = [(keys, values, base, base)]
        slots += [(item, item, 0, group_heads) for item in got]
        slots += [(left_k, left_v, base, base)]
        slots += [(item[0], item[0], 0, group_heads) for item in forwarded]
        slots += [(right_k, right_v, base, base)]
        slots += [(item[1], item[1], 0, group_heads) for item in forwarded]
        reach = lax.slice_in_dim(head_windows, base, base + group_heads, axis=0)
        window = (far_rows[None, :] <= reach[:, 0:1]) & (far_cols[None, :] <= reach[:, 1:2])
        usable = key_real[None, :, :] & window[:, :, None]
        attended = group_attention(queries, slots, usable, base, group_heads, head_dim, score_scale)
        attended = jnp.where(query_real[:, None], attended, 0)
        rows_g = lax.slice_in_dim(weight_all, g * group_width, (g + 1) * group_width, axis=0)
        part = jnp.dot(attended, rows_g, preferred_element_type=jnp.float32)
        outputs.append(part)

    projected = outputs[0]
    for part in outputs[1:]:
        projected = projected + part
    return (projected * gate[None, :]).astype(jnp.bfloat16)


def solution(mesh):
    placed = (
        P(("groups", "seq"), None),
        P(("groups", "seq"), None),
        P(("groups", "seq"), None),
        P(("groups", "seq")),
        P(),
        P("seq", None),
        P("groups"),
    )

    return jax.shard_map(
        on_device, mesh=mesh, in_specs=placed, out_specs=P(("groups", "seq"), None), check_vma=False
    )
```

```python
import math

import jax
import jax.numpy as jnp
from jax import lax
from jax.experimental import pallas as pl
from jax.sharding import PartitionSpec as P


TW = 8
SIZES = (5, 4, 3)


def group_attention(queries, slots, usable, head_base, group_heads, head_dim, score_scale):
    tile_rows, _ = queries.shape
    count = len(slots)

    def kernel(*refs):
        query = refs[0][...]
        key_refs = refs[1:1 + 2 * count:2]
        value_refs = refs[2:2 + 2 * count:2]
        mask_ref = refs[1 + 2 * count]
        out_ref = refs[-1]
        scores = []
        allowed = []
        for j in range(count):
            part = lax.dot_general(
                query, key_refs[j][...], (((1,), (1,)), ((), ())),
                preferred_element_type=jnp.float32,
            ) * score_scale
            ok = mask_ref[0, j:j + 1, :] != 0
            scores.append(jnp.where(ok, part, -1e30))
            allowed.append(ok)
        maximum = scores[0].max(axis=1, keepdims=True)
        for part in scores[1:]:
            maximum = jnp.maximum(maximum, part.max(axis=1, keepdims=True))
        exponents = [
            jnp.where(ok, jnp.exp(part - maximum), 0.0) for part, ok in zip(scores, allowed)
        ]
        denominator = exponents[0].sum(axis=1, keepdims=True)
        for part in exponents[1:]:
            denominator = denominator + part.sum(axis=1, keepdims=True)
        total = None
        for j in range(count):
            weights = (exponents[j] / denominator).astype(jnp.bfloat16)
            term = jnp.dot(weights, value_refs[j][...], preferred_element_type=jnp.float32)
            total = term if total is None else total + term
        out_ref[...] = total.astype(out_ref.dtype)

    in_specs = [pl.BlockSpec((tile_rows, head_dim), lambda h: (0, head_base + h))]
    operands = [queries]
    for key_array, value_array, key_block, value_block in slots:
        in_specs.append(pl.BlockSpec((tile_rows, head_dim), lambda h, b=key_block: (0, b + h)))
        in_specs.append(pl.BlockSpec((tile_rows, head_dim), lambda h, b=value_block: (0, b + h)))
        operands += [key_array, value_array]
    in_specs.append(pl.BlockSpec((1, count, tile_rows), lambda h: (h, 0, 0)))
    operands.append(usable.astype(jnp.int32))
    return pl.pallas_call(
        kernel,
        grid=(group_heads,),
        in_specs=in_specs,
        out_specs=pl.BlockSpec((tile_rows, head_dim), lambda h: (0, h)),
        out_shape=jax.ShapeDtypeStruct((tile_rows, group_heads * head_dim), queries.dtype),
    )(*operands)


def vertical_parts(devices, grid_rows):
    if grid_rows == 1:
        return []
    down = [(i, i + TW) for i in range(devices - TW)]
    up = [(i + TW, i) for i in range(devices - TW)]
    if grid_rows == 2:
        return [down + up]
    return [down, up]


def on_device(queries, keys, values, tile_lengths, head_windows, out_weight, gate):
    devices = lax.axis_size("seq")
    grid_rows = devices // TW
    tile_rows = queries.shape[0]
    feat_width = queries.shape[1]
    head_count = head_windows.shape[0]
    head_dim = feat_width // head_count
    score_scale = 1.0 / math.sqrt(head_dim)
    sizes = SIZES if sum(SIZES) == head_count else (head_count,)
    starts = [sum(sizes[:g]) for g in range(len(sizes))]

    to_right = [(i, i + 1) for i in range(devices) if i % TW < TW - 1]
    to_left = [(i + 1, i) for i in range(devices) if i % TW < TW - 1]
    sideways = lambda x: (lax.ppermute(x, "seq", to_right), lax.ppermute(x, "seq", to_left))

    weight_all = lax.all_gather(out_weight, "seq", axis=0, tiled=True)
    verticals = vertical_parts(devices, grid_rows)
    left_of = lambda pairs: [(s, r + 1) for s, r in pairs if r % TW < TW - 1]
    right_of = lambda pairs: [(s, r - 1) for s, r in pairs if r % TW > 0]
    fetch = lambda pairs: lax.ppermute(tile_lengths, "seq", pairs)
    vert_lens = [fetch(pairs) for pairs in verticals]
    column_lens = jnp.concatenate([tile_lengths] + vert_lens)
    left_lens = jnp.concatenate([fetch(to_right)] + [fetch(left_of(p)) for p in verticals])
    right_lens = jnp.concatenate([fetch(to_left)] + [fetch(right_of(p)) for p in verticals])
    left_kv, right_kv = sideways(jnp.concatenate([keys, values], axis=1))

    positions = jnp.arange(tile_rows, dtype=jnp.int32)
    query_real = positions < tile_lengths[0]
    rows = [0] + [1] * len(verticals)
    far_rows = jnp.array(rows * 3, jnp.int32)
    far_cols = jnp.array([0] * len(rows) + [1] * (2 * len(rows)), jnp.int32)
    length_stack = jnp.concatenate([column_lens, left_lens, right_lens])
    key_real = positions[None, :] < length_stack[:, None]

    def chunk(x, g):
        return lax.slice_in_dim(x, starts[g] * head_dim, (starts[g] + sizes[g]) * head_dim, axis=1)

    outputs = []
    previous = None
    for g in range(len(sizes)):
        group_heads = sizes[g]
        own = jnp.concatenate([chunk(keys, g), chunk(values, g)], axis=1)
        if previous is not None:
            own, _ = lax.optimization_barrier((own, previous))
        got = [lax.ppermute(own, "seq", pairs) for pairs in verticals]
        if got:
            previous = got[-1]
        forwarded = [sideways(item) for item in got]
        base = starts[g]
        slots = [(keys, values, base, base)]
        slots += [(item, item, 0, group_heads) for item in got]
        slots += [(left_kv, left_kv, base, head_count + base)]
        slots += [(item[0], item[0], 0, group_heads) for item in forwarded]
        slots += [(right_kv, right_kv, base, head_count + base)]
        slots += [(item[1], item[1], 0, group_heads) for item in forwarded]
        reach = lax.slice_in_dim(head_windows, base, base + group_heads, axis=0)
        window = (far_rows[None, :] <= reach[:, 0:1]) & (far_cols[None, :] <= reach[:, 1:2])
        usable = key_real[None, :, :] & window[:, :, None]
        attended = group_attention(queries, slots, usable, base, group_heads, head_dim, score_scale)
        outputs.append(jnp.where(query_real[:, None], attended, 0))

    attended_all = jnp.concatenate(outputs, axis=1)
    projected = jnp.dot(attended_all, weight_all, preferred_element_type=jnp.float32)
    return (projected * gate[None, :]).astype(jnp.bfloat16)


def solution(mesh):
    placed = (
        P(("groups", "seq"), None),
        P(("groups", "seq"), None),
        P(("groups", "seq"), None),
        P(("groups", "seq")),
        P(),
        P("seq", None),
        P("groups"),
    )

    return jax.shard_map(
        on_device, mesh=mesh, in_specs=placed, out_specs=P(("groups", "seq"), None), check_vma=False
    )
```

```python
import math

import jax
import jax.numpy as jnp
from jax import lax
from jax.experimental import pallas as pl
from jax.sharding import PartitionSpec as P


TW = 8
SIZES = (4, 5, 3)


def group_attention(queries, slots, usable, head_base, group_heads, head_dim, score_scale):
    tile_rows, _ = queries.shape
    count = len(slots)

    def kernel(*refs):
        query = refs[0][...]
        key_refs = refs[1:1 + 2 * count:2]
        value_refs = refs[2:2 + 2 * count:2]
        mask_ref = refs[1 + 2 * count]
        out_ref = refs[-1]
        scores = []
        allowed = []
        for j in range(count):
            part = lax.dot_general(
                query, key_refs[j][...], (((1,), (1,)), ((), ())),
                preferred_element_type=jnp.float32,
            ) * score_scale
            ok = mask_ref[0, j:j + 1, :] != 0
            scores.append(jnp.where(ok, part, -1e30))
            allowed.append(ok)
        maximum = scores[0].max(axis=1, keepdims=True)
        for part in scores[1:]:
            maximum = jnp.maximum(maximum, part.max(axis=1, keepdims=True))
        exponents = [
            jnp.where(ok, jnp.exp(part - maximum), 0.0) for part, ok in zip(scores, allowed)
        ]
        denominator = exponents[0].sum(axis=1, keepdims=True)
        for part in exponents[1:]:
            denominator = denominator + part.sum(axis=1, keepdims=True)
        total = None
        for j in range(count):
            weights = (exponents[j] / denominator).astype(jnp.bfloat16)
            term = jnp.dot(weights, value_refs[j][...], preferred_element_type=jnp.float32)
            total = term if total is None else total + term
        out_ref[...] = total.astype(out_ref.dtype)

    in_specs = [pl.BlockSpec((tile_rows, head_dim), lambda h: (0, head_base + h))]
    operands = [queries]
    for key_array, value_array, key_block, value_block in slots:
        in_specs.append(pl.BlockSpec((tile_rows, head_dim), lambda h, b=key_block: (0, b + h)))
        in_specs.append(pl.BlockSpec((tile_rows, head_dim), lambda h, b=value_block: (0, b + h)))
        operands += [key_array, value_array]
    in_specs.append(pl.BlockSpec((1, count, tile_rows), lambda h: (h, 0, 0)))
    operands.append(usable.astype(jnp.int32))
    return pl.pallas_call(
        kernel,
        grid=(group_heads,),
        in_specs=in_specs,
        out_specs=pl.BlockSpec((tile_rows, head_dim), lambda h: (0, h)),
        out_shape=jax.ShapeDtypeStruct((tile_rows, group_heads * head_dim), queries.dtype),
    )(*operands)


def vertical_parts(devices, grid_rows):
    if grid_rows == 1:
        return []
    down = [(i, i + TW) for i in range(devices - TW)]
    up = [(i + TW, i) for i in range(devices - TW)]
    if grid_rows == 2:
        return [down + up]
    return [down, up]


def on_device(queries, keys, values, tile_lengths, head_windows, out_weight, gate):
    devices = lax.axis_size("seq")
    grid_rows = devices // TW
    tile_rows = queries.shape[0]
    feat_width = queries.shape[1]
    head_count = head_windows.shape[0]
    head_dim = feat_width // head_count
    score_scale = 1.0 / math.sqrt(head_dim)
    sizes = SIZES if sum(SIZES) == head_count else (head_count,)
    starts = [sum(sizes[:g]) for g in range(len(sizes))]

    to_right = [(i, i + 1) for i in range(devices) if i % TW < TW - 1]
    to_left = [(i + 1, i) for i in range(devices) if i % TW < TW - 1]
    sideways = lambda x: (lax.ppermute(x, "seq", to_right), lax.ppermute(x, "seq", to_left))

    weight_all = lax.all_gather(out_weight, "seq", axis=0, tiled=True)
    verticals = vertical_parts(devices, grid_rows)
    left_of = lambda pairs: [(s, r + 1) for s, r in pairs if r % TW < TW - 1]
    right_of = lambda pairs: [(s, r - 1) for s, r in pairs if r % TW > 0]
    fetch = lambda pairs: lax.ppermute(tile_lengths, "seq", pairs)
    vert_lens = [fetch(pairs) for pairs in verticals]
    column_lens = jnp.concatenate([tile_lengths] + vert_lens)
    left_lens = jnp.concatenate([fetch(to_right)] + [fetch(left_of(p)) for p in verticals])
    right_lens = jnp.concatenate([fetch(to_left)] + [fetch(right_of(p)) for p in verticals])
    (left_k, left_v), (right_k, right_v) = sideways((keys, values))

    positions = jnp.arange(tile_rows, dtype=jnp.int32)
    query_real = positions < tile_lengths[0]
    rows = [0] + [1] * len(verticals)
    far_rows = jnp.array(rows * 3, jnp.int32)
    far_cols = jnp.array([0] * len(rows) + [1] * (2 * len(rows)), jnp.int32)
    length_stack = jnp.concatenate([column_lens, left_lens, right_lens])
    key_real = positions[None, :] < length_stack[:, None]

    def chunk(x, g):
        return lax.slice_in_dim(x, starts[g] * head_dim, (starts[g] + sizes[g]) * head_dim, axis=1)

    outputs = []
    previous = None
    for g in range(len(sizes)):
        group_heads = sizes[g]
        own = jnp.concatenate([chunk(keys, g), chunk(values, g)], axis=1)
        if previous is not None:
            own, _ = lax.optimization_barrier((own, previous))
        got = [lax.ppermute(own, "seq", pairs) for pairs in verticals]
        if got:
            previous = got[-1]
        forwarded = [sideways(item) for item in got]
        base = starts[g]
        slots = [(keys, values, base, base)]
        slots += [(item, item, 0, group_heads) for item in got]
        slots += [(left_k, left_v, base, base)]
        slots += [(item[0], item[0], 0, group_heads) for item in forwarded]
        slots += [(right_k, right_v, base, base)]
        slots += [(item[1], item[1], 0, group_heads) for item in forwarded]
        reach = lax.slice_in_dim(head_windows, base, base + group_heads, axis=0)
        window = (far_rows[None, :] <= reach[:, 0:1]) & (far_cols[None, :] <= reach[:, 1:2])
        usable = key_real[None, :, :] & window[:, :, None]
        attended = group_attention(queries, slots, usable, base, group_heads, head_dim, score_scale)
        outputs.append(jnp.where(query_real[:, None], attended, 0))

    attended_all = jnp.concatenate(outputs, axis=1)
    projected = jnp.dot(attended_all, weight_all, preferred_element_type=jnp.float32)
    return (projected * gate[None, :]).astype(jnp.bfloat16)


def solution(mesh):
    placed = (
        P(("groups", "seq"), None),
        P(("groups", "seq"), None),
        P(("groups", "seq"), None),
        P(("groups", "seq")),
        P(),
        P("seq", None),
        P("groups"),
    )

    return jax.shard_map(
        on_device, mesh=mesh, in_specs=placed, out_specs=P(("groups", "seq"), None), check_vma=False
    )
```
